512 devices in a mesh: chain: 64 (over y, z), cross: 8 (over x, core).
Axes of the slice: x: 4, y: 8, z: 8, core: 2. Of those that a mesh axis runs over, the one named last changes fastest.
Arguments:
- right_side: bfloat16 [64, 1024, 512], P('chain', 'cross'), may hold values from -6 to 6
- self_factor: bfloat16 [6, 64, 1024, 1024], P(None, 'chain', 'cross')
- lower_factor: bfloat16 [6, 64, 1024, 1024], P(None, 'chain', 'cross'), may hold values from -0.078125 to 0.078125
- upper_factor: bfloat16 [6, 64, 1024, 1024], P(None, 'chain', 'cross'), may hold values from -0.078125 to 0.078125
Outputs:
- solution: bfloat16 [64, 1024, 512], P('chain', 'cross')
The draws below stay inside these ranges and needn't reach their ends.
All inputs are finite; a program needn't handle non-finite values.
Results may differ from the reference program's by a relative error of at most 0.014.
Values may be sent and summed in bfloat16 or wider, within the bound.
No kernel may reach another device: no remote copies, remote signals or barrier semaphores. Data moves between devices by JAX's collectives and lax.ppermute only.
A program may use at most 64 MiB of HBM per device.

```python
import math
import jax
import jax.numpy as jnp

M = 1024
R = 512
PARTS_SIZE = 64
LEVELS = 6


def draw_self_factor(key, part):
    key_diag, key_off = jax.random.split(key)
    shape = (LEVELS, PARTS_SIZE, M, M)
    diag = jax.random.uniform(key_diag, (LEVELS, PARTS_SIZE, M, 1), jnp.float32, 0.4, 0.9)
    off = jax.random.normal(key_off, shape, jnp.float32) * (0.5 / math.sqrt(M))
    rows = jnp.arange(M)[:, None]
    cols = jnp.arange(M)[None, :]
    eye = (rows == cols).astype(jnp.float32)
    return (off + eye * diag).astype(jnp.bfloat16)


def block_scale(key, dims, cuts, smallest, top_value):
    factor_of = 1.0
    for axis_at, shards_of in cuts:
        steps = jax.random.uniform(jax.random.fold_in(jax.random.fold_in(key, 6), axis_at), (shards_of,), jnp.float32, smallest / len(cuts), top_value / len(cuts))
        factor_of = factor_of * jnp.repeat(jnp.exp(steps), dims[axis_at] // shards_of).reshape((-1,) + (1,) * (len(dims) - 1 - axis_at))
    return factor_of


def normal_values(key, dims, scale, reach, pieces=(), kind=jnp.bfloat16):
    array = scale * jax.random.normal(key, dims, jnp.float32)
    if pieces:
        array = array * block_scale(key, dims, pieces, -0.22, 0.18)
    return jnp.clip(array, -reach, reach).astype(kind)


def setup_inputs(seed: int = 0) -> dict:
    streams_of = jax.random.split(jax.random.key(seed), 5)
    return {
        "right_side": normal_values(streams_of[0], (PARTS_SIZE, M, R), 1.0, 6.0, ((0, 64), (1, 8))),
        "self_factor": draw_self_factor(jax.random.fold_in(streams_of[4], 71), 0),
        "lower_factor": normal_values(streams_of[2], (LEVELS, PARTS_SIZE, M, M), (5 * M) ** -0.5, 0.078125, ((1, 64), (2, 8))),
        "upper_factor": normal_values(streams_of[3], (LEVELS, PARTS_SIZE, M, M), (5 * M) ** -0.5, 0.078125, ((1, 64), (2, 8))),
    }


def reference(right_side, self_factor, lower_factor, upper_factor):
    current = right_side
    for level in range(LEVELS):
        dist = 2 ** level
        empty = jnp.zeros((dist, M, R), jnp.bfloat16)
        lower = jnp.concatenate([empty, current[:PARTS_SIZE - dist]], axis=0)
        upper = jnp.concatenate([current[dist:], empty], axis=0)
        total = jnp.einsum("pij,pjr->pir", self_factor[level].astype(jnp.float32), current.astype(jnp.float32))
        total = total - jnp.einsum("pij,pjr->pir", lower_factor[level].astype(jnp.float32), lower.astype(jnp.float32))
        total = total - jnp.einsum("pij,pjr->pir", upper_factor[level].astype(jnp.float32), upper.astype(jnp.float32))
        current = total.astype(jnp.bfloat16)
    return current
```

```python
import jax
import jax.numpy as jnp
from jax import lax
from jax.sharding import PartitionSpec as P


def shifted(value, axis, steps):
    count = lax.axis_size(axis)
    initial, last = (max(0, -steps), min(count, count - steps))
    return lax.ppermute(value, axis, [(source, source + steps) for source in range(initial, last)])


def slot_sources(chips):
    del chips
    return [(0, 0), (0, 1), (-1, 0), (-1, 1), (-2, 0), (1, 1), (1, 0), (2, 1)]


def body(right_side, self_factor, lower_factor, upper_factor):
    levels = lax.axis_size("chain").bit_length() - 1
    ncross = lax.axis_size("cross")
    chips = ncross // 2
    rows = right_side.shape[1]
    cross = lax.axis_index("cross")
    chip = cross // 2
    core = cross % 2
    sign = 1 - 2 * core

    slots = slot_sources(chips)
    source = jnp.stack(
        [2 * ((chip + off * sign) % chips) + jnp.where(other == 1, 1 - core, core) for off, other in slots]
    )

    signed = jnp.stack([self_factor[:, 0], -lower_factor[:, 0], -upper_factor[:, 0]], axis=2)
    signed = signed.reshape(levels, rows, 3, ncross, rows)
    signed = jnp.take(signed, source, axis=3)
    signed = signed.transpose(0, 1, 3, 2, 4)

    swap = [(2 * c + b, 2 * c + 1 - b) for c in range(chips) for b in range(2)]
    ring = [(2 * c, 2 * ((c + 1) % chips)) for c in range(chips)] + [
        (2 * c + 1, 2 * ((c - 1) % chips) + 1) for c in range(chips)
    ]

    def part(mat, pieces):
        n = pieces.shape[0]
        return jnp.einsum(
            "ijbk,jbkr->ir",
            mat.reshape(rows, n, 3, rows),
            pieces,
            preferred_element_type=jnp.float32,
        )

    current = right_side[0]
    for level in range(levels):
        dist = 2**level
        lower = shifted(current, "chain", dist)
        upper = shifted(current, "chain", -dist)
        own = jnp.stack([current, lower, upper])
        other = lax.ppermute(own, "cross", swap)
        first = lax.ppermute(own, "cross", ring)
        second = lax.ppermute(jnp.stack([other, first]), "cross", ring)
        third = lax.ppermute(jnp.stack([first, second[0], second[1]]), "cross", swap)
        mat = signed[level].reshape(rows, ncross * 3 * rows)
        w = 3 * rows
        total = part(mat[:, : 3 * w], jnp.stack([own, other, first]))
        total = total + part(mat[:, 3 * w : 5 * w], second)
        total = total + part(mat[:, 5 * w :], third)
        current = total.astype(jnp.bfloat16)
    return current[None]


def solution(mesh):
    return jax.shard_map(
        body,
        mesh=mesh,
        in_specs=(
            P("chain", "cross", None),
            P(None, "chain", "cross", None),
            P(None, "chain", "cross", None),
            P(None, "chain", "cross", None),
        ),
        out_specs=P("chain", "cross", None),
        check_vma=False,
    )
```

```python
import jax
import jax.numpy as jnp
from jax import lax
from jax.sharding import PartitionSpec as P


def shifted(value, axis, steps):
    count = lax.axis_size(axis)
    initial, last = (max(0, -steps), min(count, count - steps))
    return lax.ppermute(value, axis, [(source, source + steps) for source in range(initial, last)])


OFFSETS = (0, -1, 1, 2)


def body(right_side, self_factor, lower_factor, upper_factor):
    levels = lax.axis_size("chain").bit_length() - 1
    ncross = lax.axis_size("cross")
    chips = ncross // 2
    rows = right_side.shape[1]
    cross = lax.axis_index("cross")
    chip = cross // 2
    core = cross % 2

    def columns_for(which_core):
        return jnp.stack([2 * ((chip + off) % chips) + which_core for off in OFFSETS])

    signed = jnp.stack([self_factor[:, 0], -lower_factor[:, 0], -upper_factor[:, 0]], axis=2)
    signed = signed.reshape(levels, rows, 3, ncross, rows)

    def pick(which_core):
        part = jnp.take(signed, columns_for(which_core), axis=3)
        return part.transpose(0, 1, 3, 2, 4)

    mine = pick(core)
    swap = [(2 * c + b, 2 * c + 1 - b) for c in range(chips) for b in range(2)]
    theirs = lax.ppermute(pick(1 - core), "cross", swap)

    def same_core(offset):
        return [(2 * c + b, 2 * ((c + offset) % chips) + b) for c in range(chips) for b in range(2)]

    def partial(mat, pieces):
        total = None
        for j, piece in enumerate(pieces):
            term = jnp.einsum("ibk,bkr->ir", mat[:, j], piece, preferred_element_type=jnp.float32)
            total = term if total is None else total + term
        return total

    current = right_side[0]
    for level in range(levels):
        dist = 2**level
        lower = shifted(current, "chain", dist)
        upper = shifted(current, "chain", -dist)
        own = jnp.stack([current, lower, upper])
        pieces = [own] + [lax.ppermute(own, "cross", same_core(-off)) for off in OFFSETS[1:]]
        given = lax.ppermute(partial(theirs[level], pieces), "cross", swap)
        total = partial(mine[level], pieces) + given
        current = total.astype(jnp.bfloat16)
    return current[None]


def solution(mesh):
    return jax.shard_map(
        body,
        mesh=mesh,
        in_specs=(
            P("chain", "cross", None),
            P(None, "chain", "cross", None),
            P(None, "chain", "cross", None),
            P(None, "chain", "cross", None),
        ),
        out_specs=P("chain", "cross", None),
        check_vma=False,
    )
```

```python
import jax
import jax.numpy as jnp
from jax import lax
from jax.sharding import PartitionSpec as P


OFFSETS = (0, -1, 1, 2)


def body(right_side, self_factor, lower_factor, upper_factor):
    nchain = lax.axis_size("chain")
    levels = nchain.bit_length() - 1
    ncross = lax.axis_size("cross")
    chips = ncross // 2
    rows = right_side.shape[1]
    cross = lax.axis_index("cross")
    chip = cross // 2
    core = cross % 2

    swap = [(2 * c + b, 2 * c + 1 - b) for c in range(chips) for b in range(2)]

    def same_core(offset):
        return [(2 * c + b, 2 * ((c + offset) % chips) + b) for c in range(chips) for b in range(2)]

    def neighbour_pairs(dist):
        pairs = []
        for p in range(nchain):
            for c in range(ncross):
                q = p + dist if c % 2 == 0 else p - dist
                if 0 <= q < nchain:
                    pairs.append((p * ncross + c, q * ncross + c))
        return pairs

    own = right_side[0]
    pair = jnp.concatenate([own, lax.ppermute(own, "cross", swap)])
    first = lax.ppermute(pair, ("chain", "cross"), neighbour_pairs(1))

    first, self_factor, lower_factor, upper_factor = lax.optimization_barrier(
        (first, self_factor, lower_factor, upper_factor)
    )
    s_blocks = self_factor[:, 0].reshape(levels, rows, ncross, rows)
    neighbour = jnp.where(core == 0, lower_factor[:, 0], upper_factor[:, 0]).reshape(levels, rows, ncross, rows)
    given = jnp.where(core == 0, upper_factor[:, 0], lower_factor[:, 0]).reshape(levels, rows, ncross, rows)

    def arrange(s_part, n_part, which_core):
        slot_chips = [(chip + off) % chips for off in OFFSETS]
        s_idx = jnp.stack([2 * c + which_core for c in slot_chips])
        n_idx = jnp.stack([2 * c + t for c in slot_chips for t in (which_core, 1 - which_core)])
        s_sel = jnp.take(s_part, s_idx, axis=2)[:, :, :, None]
        n_sel = jnp.take(n_part, n_idx, axis=2).reshape(levels, rows, len(OFFSETS), 2, rows)
        return jnp.concatenate([s_sel, -n_sel], axis=3)

    mine = arrange(s_blocks, neighbour, core)
    theirs = lax.ppermute(arrange(s_blocks, given, 1 - core), "cross", swap)

    def partial(mat, pieces):
        total = None
        for j, piece in enumerate(pieces):
            term = jnp.einsum(
                "ibk,bkr->ir", mat[:, j], piece.reshape(3, rows, -1), preferred_element_type=jnp.float32
            )
            total = term if total is None else total + term
        return total

    for level in range(levels):
        near = first if level == 0 else lax.ppermute(pair, ("chain", "cross"), neighbour_pairs(2**level))
        piece = jnp.concatenate([pair[:rows], near])
        pieces = [piece] + [lax.ppermute(piece, "cross", same_core(-off)) for off in OFFSETS[1:]]
        mine_part = partial(mine[level], pieces)
        their_part = partial(theirs[level], pieces)
        back = lax.ppermute(jnp.stack([mine_part, their_part]), "cross", swap)
        pair = jnp.concatenate([mine_part + back[1], their_part + back[0]]).astype(jnp.bfloat16)
    return pair[None, :rows]


def solution(mesh):
    return jax.shard_map(
        body,
        mesh=mesh,
        in_specs=(
            P("chain", "cross", None),
            P(None, "chain", "cross", None),
            P(None, "chain", "cross", None),
            P(None, "chain", "cross", None),
        ),
        out_specs=P("chain", "cross", None),
        check_vma=False,
    )
```

```python
import jax
import jax.numpy as jnp
from jax import lax
from jax.sharding import PartitionSpec as P


def shifted(value, axis, steps):
    count = lax.axis_size(axis)
    initial, last = (max(0, -steps), min(count, count - steps))
    return lax.ppermute(value, axis, [(source, source + steps) for source in range(initial, last)])


OFFSETS = (0, -1, 1, 2)


def body(right_side, self_factor, lower_factor, upper_factor):
    levels = lax.axis_size("chain").bit_length() - 1
    ncross = lax.axis_size("cross")
    chips = ncross // 2
    rows = right_side.shape[1]
    cross = lax.axis_index("cross")
    chip = cross // 2
    core = cross % 2

    def columns_for(which_core):
        return jnp.stack([2 * ((chip + off) % chips) + which_core for off in OFFSETS])

    def arrange(level, which_core):
        signed = jnp.stack([self_factor[level, 0], -lower_factor[level, 0], -upper_factor[level, 0]], axis=1)
        signed = signed.reshape(rows, 3, ncross, rows)
        part = jnp.take(signed, columns_for(which_core), axis=2)
        return part.transpose(0, 2, 1, 3)

    swap = [(2 * c + b, 2 * c + 1 - b) for c in range(chips) for b in range(2)]
    theirs = lax.ppermute(arrange(0, 1 - core), "cross", swap)

    def same_core(offset):
        return [(2 * c + b, 2 * ((c + offset) % chips) + b) for c in range(chips) for b in range(2)]

    def partial(mat, pieces):
        total = None
        for j, piece in enumerate(pieces):
            term = jnp.einsum("ibk,bkr->ir", mat[:, j], piece, preferred_element_type=jnp.float32)
            total = term if total is None else total + term
        return total

    current = right_side[0]
    for level in range(levels):
        dist = 2**level
        lower = shifted(current, "chain", dist)
        upper = shifted(current, "chain", -dist)
        own = jnp.stack([current, lower, upper])
        pieces = [own] + [lax.ppermute(own, "cross", same_core(-off)) for off in OFFSETS[1:]]
        their_part = partial(theirs, pieces)
        if level + 1 < levels:
            given, theirs = lax.ppermute((their_part, arrange(level + 1, 1 - core)), "cross", swap)
        else:
            given = lax.ppermute(their_part, "cross", swap)
        total = partial(arrange(level, core), pieces) + given
        current = total.astype(jnp.bfloat16)
    return current[None]


def solution(mesh):
    return jax.shard_map(
        body,
        mesh=mesh,
        in_specs=(
            P("chain", "cross", None),
            P(None, "chain", "cross", None),
            P(None, "chain", "cross", None),
            P(None, "chain", "cross", None),
        ),
        out_specs=P("chain", "cross", None),
        check_vma=False,
    )
```

```python
import jax
import jax.numpy as jnp
from jax import lax
from jax.sharding import PartitionSpec as P


def shifted(value, axis, steps):
    count = lax.axis_size(axis)
    initial, last = (max(0, -steps), min(count, count - steps))
    return lax.ppermute(value, axis, [(source, source + steps) for source in range(initial, last)])


OFFSETS = (0, -1, 1, 2)


def body(right_side, self_factor, lower_factor, upper_factor):
    levels = lax.axis_size("chain").bit_length() - 1
    ncross = lax.axis_size("cross")
    chips = ncross // 2
    rows = right_side.shape[1]
    cross = lax.axis_index("cross")
    chip = cross // 2
    core = cross % 2

    def columns_for(which_core):
        return jnp.stack([2 * ((chip + off) % chips) + which_core for off in OFFSETS])

    blocks = [f[:, 0].reshape(levels, rows, ncross, rows) for f in (self_factor, lower_factor, upper_factor)]

    def pick(which_core):
        idx = columns_for(which_core)
        parts = [jnp.take(blocks[0], idx, axis=2)] + [-jnp.take(f, idx, axis=2) for f in blocks[1:]]
        return jnp.stack(parts, axis=3)

    mine = pick(core)
    swap = [(2 * c + b, 2 * c + 1 - b) for c in range(chips) for b in range(2)]
    theirs = lax.ppermute(pick(1 - core), "cross", swap)

    def same_core(offset):
        return [(2 * c + b, 2 * ((c + offset) % chips) + b) for c in range(chips) for b in range(2)]

    def partial(mat, pieces):
        total = None
        for j, piece in enumerate(pieces):
            term = jnp.einsum("ibk,bkr->ir", mat[:, j], piece, preferred_element_type=jnp.float32)
            total = term if total is None else total + term
        return total

    current = right_side[0]
    for level in range(levels):
        dist = 2**level
        lower = shifted(current, "chain", dist)
        upper = shifted(current, "chain", -dist)
        own = jnp.stack([current, lower, upper])
        pieces = [own] + [lax.ppermute(own, "cross", same_core(-off)) for off in OFFSETS[1:]]
        given = lax.ppermute(partial(theirs[level], pieces), "cross", swap)
        total = partial(mine[level], pieces) + given
        current = total.astype(jnp.bfloat16)
    return current[None]


def solution(mesh):
    return jax.shard_map(
        body,
        mesh=mesh,
        in_specs=(
            P("chain", "cross", None),
            P(None, "chain", "cross", None),
            P(None, "chain", "cross", None),
            P(None, "chain", "cross", None),
        ),
        out_specs=P("chain", "cross", None),
        check_vma=False,
    )
```

```python
import jax
import jax.numpy as jnp
from jax import lax
from jax.sharding import PartitionSpec as P


def shifted(value, axis, steps):
    count = lax.axis_size(axis)
    initial, last = (max(0, -steps), min(count, count - steps))
    return lax.ppermute(value, axis, [(source, source + steps) for source in range(initial, last)])


OFFSETS = (0, -1, 1, 2)


def body(right_side, self_factor, lower_factor, upper_factor):
    levels = lax.axis_size("chain").bit_length() - 1
    ncross = lax.axis_size("cross")
    chips = ncross // 2
    rows = right_side.shape[1]
    cross = lax.axis_index("cross")
    chip = cross // 2
    core = cross % 2

    def columns_for(which_core):
        return jnp.stack([2 * ((chip + off) % chips) + which_core for off in OFFSETS])

    swap = [(2 * c + b, 2 * c + 1 - b) for c in range(chips) for b in range(2)]

    def arranged(factors, which_core):
        count = factors[0].shape[0]
        signed = jnp.stack([factors[0][:, 0], -factors[1][:, 0], -factors[2][:, 0]], axis=2)
        signed = signed.reshape(count, rows, 3, ncross, rows)
        part = jnp.take(signed, columns_for(which_core), axis=3)
        return part.transpose(0, 1, 3, 2, 4)

    def prepare(factors):
        return arranged(factors, core), lax.ppermute(arranged(factors, 1 - core), "cross", swap)

    factors = (self_factor, lower_factor, upper_factor)
    mine, theirs = prepare(tuple(f[:1] for f in factors))

    def same_core(offset):
        return [(2 * c + b, 2 * ((c + offset) % chips) + b) for c in range(chips) for b in range(2)]

    def partial(mat, pieces):
        total = None
        for j, piece in enumerate(pieces):
            term = jnp.einsum("ibk,bkr->ir", mat[:, j], piece, preferred_element_type=jnp.float32)
            total = term if total is None else total + term
        return total

    current = right_side[0]
    for level in range(levels):
        dist = 2**level
        lower = shifted(current, "chain", dist)
        upper = shifted(current, "chain", -dist)
        own = jnp.stack([current, lower, upper])
        pieces = [own] + [lax.ppermute(own, "cross", same_core(-off)) for off in OFFSETS[1:]]
        if level == 0 and levels > 1:
            pieces, rest = lax.optimization_barrier((pieces, tuple(f[1:] for f in factors)))
            later_mine, later_theirs = prepare(rest)
        at = 0 if level == 0 else level - 1
        use_mine, use_theirs = (mine, theirs) if level == 0 else (later_mine, later_theirs)
        given = lax.ppermute(partial(use_theirs[at], pieces), "cross", swap)
        total = partial(use_mine[at], pieces) + given
        current = total.astype(jnp.bfloat16)
    return current[None]


def solution(mesh):
    return jax.shard_map(
        body,
        mesh=mesh,
        in_specs=(
            P("chain", "cross", None),
            P(None, "chain", "cross", None),
            P(None, "chain", "cross", None),
            P(None, "chain", "cross", None),
        ),
        out_specs=P("chain", "cross", None),
        check_vma=False,
    )
```

```python
import jax
import jax.numpy as jnp
from jax import lax
from jax.sharding import PartitionSpec as P


def shifted(value, axis, steps):
    count = lax.axis_size(axis)
    initial, last = (max(0, -steps), min(count, count - steps))
    return lax.ppermute(value, axis, [(source, source + steps) for source in range(initial, last)])


OFFSETS = (0, -1, 1, 2)


def body(right_side, self_factor, lower_factor, upper_factor):
    levels = lax.axis_size("chain").bit_length() - 1
    ncross = lax.axis_size("cross")
    chips = ncross // 2
    rows = right_side.shape[1]
    cross = lax.axis_index("cross")
    chip = cross // 2
    core = cross % 2

    def columns_for(which_core):
        return jnp.stack([2 * ((chip + off) % chips) + which_core for off in OFFSETS])

    signed = jnp.stack([self_factor[:, 0], -lower_factor[:, 0], -upper_factor[:, 0]], axis=2)
    signed = signed.reshape(levels, rows, 3, ncross, rows)

    def pick(which_core):
        part = jnp.take(signed, columns_for(which_core), axis=3)
        return part.transpose(0, 1, 3, 2, 4)

    def pick_level(level, which_core):
        part = jnp.take(signed[level], columns_for(which_core), axis=2)
        return part.transpose(0, 2, 1, 3)

    swap = [(2 * c + b, 2 * c + 1 - b) for c in range(chips) for b in range(2)]
    theirs = lax.ppermute(pick(1 - core), "cross", swap)

    def same_core(offset):
        return [(2 * c + b, 2 * ((c + offset) % chips) + b) for c in range(chips) for b in range(2)]

    def partial(mat, pieces):
        total = None
        for j, piece in enumerate(pieces):
            term = jnp.einsum("ibk,bkr->ir", mat[:, j], piece, preferred_element_type=jnp.float32)
            total = term if total is None else total + term
        return total

    current = right_side[0]
    for level in range(levels):
        dist = 2**level
        lower = shifted(current, "chain", dist)
        upper = shifted(current, "chain", -dist)
        own = jnp.stack([current, lower, upper])
        pieces = [own] + [lax.ppermute(own, "cross", same_core(-off)) for off in OFFSETS[1:]]
        given = lax.ppermute(partial(theirs[level], pieces), "cross", swap)
        total = partial(pick_level(level, core), pieces) + given
        current = total.astype(jnp.bfloat16)
    return current[None]


def solution(mesh):
    return jax.shard_map(
        body,
        mesh=mesh,
        in_specs=(
            P("chain", "cross", None),
            P(None, "chain", "cross", None),
            P(None, "chain", "cross", None),
            P(None, "chain", "cross", None),
        ),
        out_specs=P("chain", "cross", None),
        check_vma=False,
    )
```

```python
import jax
import jax.numpy as jnp
from jax import lax
from jax.sharding import PartitionSpec as P


def shifted(value, axis, steps):
    count = lax.axis_size(axis)
    initial, last = (max(0, -steps), min(count, count - steps))
    return lax.ppermute(value, axis, [(source, source + steps) for source in range(initial, last)])


OFFSETS = (0, -1, 1, 2)


def body(right_side, self_factor, lower_factor, upper_factor):
    levels = lax.axis_size("chain").bit_length() - 1
    ncross = lax.axis_size("cross")
    chips = ncross // 2
    rows = right_side.shape[1]
    cross = lax.axis_index("cross")
    chip = cross // 2
    core = cross % 2

    signed = jnp.stack([self_factor[:, 0], -lower_factor[:, 0], -upper_factor[:, 0]], axis=2)
    signed = signed.reshape(levels, rows, 3, chips, 2, rows)

    def core_columns(which_core):
        return lax.dynamic_index_in_dim(signed, which_core, axis=4, keepdims=False)

    swap = [(2 * c + b, 2 * c + 1 - b) for c in range(chips) for b in range(2)]
    mine = core_columns(core)
    theirs = lax.ppermute(core_columns(1 - core), "cross", swap)
    slot_chips = [(chip + off) % chips for off in OFFSETS]

    def same_core(offset):
        return [(2 * c + b, 2 * ((c + offset) % chips) + b) for c in range(chips) for b in range(2)]

    def partial(mat, pieces):
        total = None
        for j, piece in enumerate(pieces):
            block = lax.dynamic_index_in_dim(mat, slot_chips[j], axis=2, keepdims=False)
            term = jnp.einsum("ibk,bkr->ir", block, piece, preferred_element_type=jnp.float32)
            total = term if total is None else total + term
        return total

    current = right_side[0]
    for level in range(levels):
        dist = 2**level
        lower = shifted(current, "chain", dist)
        upper = shifted(current, "chain", -dist)
        own = jnp.stack([current, lower, upper])
        pieces = [own] + [lax.ppermute(own, "cross", same_core(-off)) for off in OFFSETS[1:]]
        given = lax.ppermute(partial(theirs[level], pieces), "cross", swap)
        total = partial(mine[level], pieces) + given
        current = total.astype(jnp.bfloat16)
    return current[None]


def solution(mesh):
    return jax.shard_map(
        body,
        mesh=mesh,
        in_specs=(
            P("chain", "cross", None),
            P(None, "chain", "cross", None),
            P(None, "chain", "cross", None),
            P(None, "chain", "cross", None),
        ),
        out_specs=P("chain", "cross", None),
        check_vma=False,
    )
```

```python
import jax
import jax.numpy as jnp
from jax import lax
from jax.sharding import PartitionSpec as P


def shifted(value, axis, steps):
    count = lax.axis_size(axis)
    initial, last = (max(0, -steps), min(count, count - steps))
    return lax.ppermute(value, axis, [(source, source + steps) for source in range(initial, last)])


OFFSETS = (0, -1, 1, 2)


def body(right_side, self_factor, lower_factor, upper_factor):
    levels = lax.axis_size("chain").bit_length() - 1
    ncross = lax.axis_size("cross")
    chips = ncross // 2
    rows = right_side.shape[1]
    cross = lax.axis_index("cross")
    chip = cross // 2
    core = cross % 2

    def columns_for(which_core):
        return jnp.stack([2 * ((chip + off) % chips) + which_core for off in OFFSETS])

    swap = [(2 * c + b, 2 * c + 1 - b) for c in range(chips) for b in range(2)]

    def arranged(factors, which_core):
        count = factors[0].shape[0]
        signed = jnp.stack([factors[0][:, 0], -factors[1][:, 0], -factors[2][:, 0]], axis=2)
        signed = signed.reshape(count, rows, 3, ncross, rows)
        part = jnp.take(signed, columns_for(which_core), axis=3)
        return part.transpose(0, 1, 3, 2, 4)

    def prepare(factors):
        return arranged(factors, core), lax.ppermute(arranged(factors, 1 - core), "cross", swap)

    factors = (self_factor, lower_factor, upper_factor)
    mine, theirs = prepare(tuple(f[:1] for f in factors))

    def same_core(offset):
        return [(2 * c + b, 2 * ((c + offset) % chips) + b) for c in range(chips) for b in range(2)]

    def partial(mat, pieces):
        total = None
        for j, piece in enumerate(pieces):
            term = jnp.einsum("ibk,bkr->ir", mat[:, j], piece, preferred_element_type=jnp.float32)
            total = term if total is None else total + term
        return total

    current = right_side[0]
    for level in range(levels):
        dist = 2**level
        lower = shifted(current, "chain", dist)
        upper = shifted(current, "chain", -dist)
        if level == 0 and levels > 1:
            lower, upper, rest = lax.optimization_barrier((lower, upper, tuple(f[1:] for f in factors)))
            later_mine, later_theirs = prepare(rest)
        own = jnp.stack([current, lower, upper])
        pieces = [own] + [lax.ppermute(own, "cross", same_core(-off)) for off in OFFSETS[1:]]
        at = 0 if level == 0 else level - 1
        use_mine, use_theirs = (mine, theirs) if level == 0 else (later_mine, later_theirs)
        given = lax.ppermute(partial(use_theirs[at], pieces), "cross", swap)
        total = partial(use_mine[at], pieces) + given
        current = total.astype(jnp.bfloat16)
    return current[None]


def solution(mesh):
    return jax.shard_map(
        body,
        mesh=mesh,
        in_specs=(
            P("chain", "cross", None),
            P(None, "chain", "cross", None),
            P(None, "chain", "cross", None),
            P(None, "chain", "cross", None),
        ),
        out_specs=P("chain", "cross", None),
        check_vma=False,
    )
```

```python
import jax
import jax.numpy as jnp
from jax import lax
from jax.sharding import PartitionSpec as P


def shifted(value, axis, steps):
    count = lax.axis_size(axis)
    initial, last = (max(0, -steps), min(count, count - steps))
    return lax.ppermute(value, axis, [(source, source + steps) for source in range(initial, last)])


OFFSETS = (0, -1, 1, 2)


def body(right_side, self_factor, lower_factor, upper_factor):
    levels = lax.axis_size("chain").bit_length() - 1
    ncross = lax.axis_size("cross")
    chips = ncross // 2
    rows = right_side.shape[1]
    cross = lax.axis_index("cross")
    chip = cross // 2
    core = cross % 2

    def columns_for(which_core):
        return jnp.stack([2 * ((chip + off) % chips) + which_core for off in OFFSETS])

    factors = [f[:, 0] for f in (self_factor, lower_factor, upper_factor)]

    def pick(which_core):
        slots = []
        for c in columns_for(which_core):
            blocks = [lax.dynamic_slice_in_dim(f, c * rows, rows, axis=2) for f in factors]
            slots.append(jnp.stack([blocks[0], -blocks[1], -blocks[2]], axis=2))
        return jnp.stack(slots, axis=2)

    mine = pick(core)
    swap = [(2 * c + b, 2 * c + 1 - b) for c in range(chips) for b in range(2)]
    theirs = lax.ppermute(pick(1 - core), "cross", swap)

    def same_core(offset):
        return [(2 * c + b, 2 * ((c + offset) % chips) + b) for c in range(chips) for b in range(2)]

    def partial(mat, pieces):
        total = None
        for j, piece in enumerate(pieces):
            term = jnp.einsum("ibk,bkr->ir", mat[:, j], piece, preferred_element_type=jnp.float32)
            total = term if total is None else total + term
        return total

    current = right_side[0]
    for level in range(levels):
        dist = 2**level
        lower = shifted(current, "chain", dist)
        upper = shifted(current, "chain", -dist)
        own = jnp.stack([current, lower, upper])
        pieces = [own] + [lax.ppermute(own, "cross", same_core(-off)) for off in OFFSETS[1:]]
        given = lax.ppermute(partial(theirs[level], pieces), "cross", swap)
        total = partial(mine[level], pieces) + given
        current = total.astype(jnp.bfloat16)
    return current[None]


def solution(mesh):
    return jax.shard_map(
        body,
        mesh=mesh,
        in_specs=(
            P("chain", "cross", None),
            P(None, "chain", "cross", None),
            P(None, "chain", "cross", None),
            P(None, "chain", "cross", None),
        ),
        out_specs=P("chain", "cross", None),
        check_vma=False,
    )
```

```python
import jax
import jax.numpy as jnp
from jax import lax
from jax.sharding import PartitionSpec as P


def shifted(value, axis, steps):
    count = lax.axis_size(axis)
    initial, last = (max(0, -steps), min(count, count - steps))
    return lax.ppermute(value, axis, [(source, source + steps) for source in range(initial, last)])


OFFSETS = (0, -1, 1, 2)


def body(right_side, self_factor, lower_factor, upper_factor):
    levels = lax.axis_size("chain").bit_length() - 1
    ncross = lax.axis_size("cross")
    chips = ncross // 2
    rows = right_side.shape[1]
    cross = lax.axis_index("cross")
    chip = cross // 2
    core = cross % 2

    def columns_for(which_core):
        return jnp.stack([2 * ((chip + off) % chips) + which_core for off in OFFSETS])

    factors = [f[:, 0] for f in (self_factor, lower_factor, upper_factor)]

    def pick(which_core):
        slots = []
        for c in columns_for(which_core):
            blocks = [lax.dynamic_slice_in_dim(f, c * rows, rows, axis=2) for f in factors]
            slots.append(jnp.stack([blocks[0], -blocks[1], -blocks[2]], axis=2))
        return jnp.stack(slots, axis=2)

    mine = pick(core)
    swap = [(2 * c + b, 2 * c + 1 - b) for c in range(chips) for b in range(2)]
    current = right_side[0]
    first = (shifted(current, "chain", 1), shifted(current, "chain", -1))
    first, given_factors = lax.optimization_barrier((first, pick(1 - core)))
    theirs = lax.ppermute(given_factors, "cross", swap)

    def same_core(offset):
        return [(2 * c + b, 2 * ((c + offset) % chips) + b) for c in range(chips) for b in range(2)]

    def partial(mat, pieces):
        total = None
        for j, piece in enumerate(pieces):
            term = jnp.einsum("ibk,bkr->ir", mat[:, j], piece, preferred_element_type=jnp.float32)
            total = term if total is None else total + term
        return total

    for level in range(levels):
        dist = 2**level
        if level == 0:
            lower, upper = first
        else:
            lower = shifted(current, "chain", dist)
            upper = shifted(current, "chain", -dist)
        own = jnp.stack([current, lower, upper])
        pieces = [own] + [lax.ppermute(own, "cross", same_core(-off)) for off in OFFSETS[1:]]
        given = lax.ppermute(partial(theirs[level], pieces), "cross", swap)
        total = partial(mine[level], pieces) + given
        current = total.astype(jnp.bfloat16)
    return current[None]


def solution(mesh):
    return jax.shard_map(
        body,
        mesh=mesh,
        in_specs=(
            P("chain", "cross", None),
            P(None, "chain", "cross", None),
            P(None, "chain", "cross", None),
            P(None, "chain", "cross", None),
        ),
        out_specs=P("chain", "cross", None),
        check_vma=False,
    )
```

```python
import jax
import jax.numpy as jnp
from jax import lax
from jax.sharding import PartitionSpec as P


def shifted(value, axis, steps):
    count = lax.axis_size(axis)
    initial, last = (max(0, -steps), min(count, count - steps))
    return lax.ppermute(value, axis, [(source, source + steps) for source in range(initial, last)])


OFFSETS = (0, -1, 1, 2)


def body(right_side, self_factor, lower_factor, upper_factor):
    levels = lax.axis_size("chain").bit_length() - 1
    ncross = lax.axis_size("cross")
    chips = ncross // 2
    rows = right_side.shape[1]
    cross = lax.axis_index("cross")
    chip = cross // 2
    core = cross % 2

    def columns_for(which_core):
        return jnp.stack([2 * ((chip + off) % chips) + which_core for off in OFFSETS])

    nchain = lax.axis_size("chain")
    last = levels - 1
    near_factor = jnp.where(lax.axis_index("chain") < nchain // 2, upper_factor[last, 0], lower_factor[last, 0])
    lower_last = jnp.concatenate([lower_factor[:last, 0], near_factor[None]])
    factors = [self_factor[:, 0], lower_last, upper_factor[:, 0]]

    def pick(which_core):
        slots = []
        for c in columns_for(which_core):
            blocks = [lax.dynamic_slice_in_dim(f, c * rows, rows, axis=2) for f in factors]
            slots.append(jnp.stack([blocks[0], -blocks[1], -blocks[2]], axis=2))
        return jnp.stack(slots, axis=2)

    mine = pick(core)
    swap = [(2 * c + b, 2 * c + 1 - b) for c in range(chips) for b in range(2)]
    current = right_side[0]
    first = (shifted(current, "chain", 1), shifted(current, "chain", -1))
    first, given_factors = lax.optimization_barrier((first, pick(1 - core)))
    theirs = lax.ppermute(given_factors, "cross", swap)

    def same_core(offset):
        return [(2 * c + b, 2 * ((c + offset) % chips) + b) for c in range(chips) for b in range(2)]

    def partial(mat, pieces):
        total = None
        for j, piece in enumerate(pieces):
            term = jnp.einsum("ibk,bkr->ir", mat[:, j], piece, preferred_element_type=jnp.float32)
            total = term if total is None else total + term
        return total

    for level in range(levels):
        dist = 2**level
        if level == 0:
            lower, upper = first
        else:
            lower = shifted(current, "chain", dist)
            upper = shifted(current, "chain", -dist)
        if level == last and 2 * dist == nchain:
            own = jnp.stack([current, lower + upper])
        else:
            own = jnp.stack([current, lower, upper])
        used = own.shape[0]
        pieces = [own] + [lax.ppermute(own, "cross", same_core(-off)) for off in OFFSETS[1:]]
        given = lax.ppermute(partial(theirs[level][:, :, :used], pieces), "cross", swap)
        total = partial(mine[level][:, :, :used], pieces) + given
        current = total.astype(jnp.bfloat16)
    return current[None]


def solution(mesh):
    return jax.shard_map(
        body,
        mesh=mesh,
        in_specs=(
            P("chain", "cross", None),
            P(None, "chain", "cross", None),
            P(None, "chain", "cross", None),
            P(None, "chain", "cross", None),
        ),
        out_specs=P("chain", "cross", None),
        check_vma=False,
    )
```
